128 devices in a mesh: dp: 16 (over z, y), vocab: 8 (over x, core).
Axes of the slice: x: 4, y: 4, z: 4, core: 2. Of those that a mesh axis runs over, the one named last changes fastest.
Arguments:
- hidden: bfloat16 [32, 512, 1024], P('dp'), may hold values from -24 to 24
- norm_gain: float32 [1024], replicated, may hold values from 0.5 to 1.5
- head: bfloat16 [1024, 32000], P('dp', 'vocab'), may hold values from -4 to 4
- targets: int32 [32, 512], P('dp'), may hold values from 0 to 31999
- lengths: int32 [32], P('dp'), may hold values from 1 to 512, 9216 in all
- groups: int32 [32, 1], P('dp'), may hold values from 0 to 3
- baseline: float32 [4], replicated, may hold values from -2 to 0
Outputs:
- logprob: float32 [32, 512], P('dp')
- entropy: float32 [32, 512], P('dp')
- group_shift: float32 [2, 4], replicated
The draws below stay inside these ranges and needn't reach their ends.
Inputs may be any that keep to these rules, and one draw needn't show every extreme that they name: `groups`: every group holds at least one sequence.
All inputs are finite; a program needn't handle non-finite values. No bound on the sum of `lengths` on one device may be relied on, other than what follows from the above.
Results may differ from the reference program's by a relative error of at most 0.00045.
The reference program's roundings to bfloat16 on the way (of `normed`) count: a program that leaves them out, or rounds other values in their place, can miss the bound.
Values may be sent and summed in bfloat16 or wider, within the bound.
No kernel may reach another device: no remote copies, remote signals or barrier semaphores. Data moves between devices by JAX's collectives and lax.ppermute only.
A program may use at most 64 MiB of HBM per device.

```python
import math
import jax
import jax.numpy as jnp
import numpy as np
from jax import lax

D = 1024
V = 32000
LEN = 512
SEQS = 32
TOTAL = 9216
GROUPS = 4


def hot_columns(key):
    chosen = jax.random.permutation(jax.random.fold_in(key, 31), V)[:8].astype(jnp.int32)
    return (chosen[:4], chosen[4:])


def head_matrix(key):
    base = jax.random.normal(jax.random.fold_in(key, 11), (D, V), jnp.float32) * 0.1
    first_cols, second_cols = hot_columns(key)
    hot_scale = 160.0 / D
    first = jax.random.normal(jax.random.fold_in(key, 13), (D, 4), jnp.float32) * hot_scale
    first = jnp.clip(first, -6.0 * hot_scale, 6.0 * hot_scale)
    noise = jax.random.normal(jax.random.fold_in(key, 14), (D, 4), jnp.float32) * (0.03 * hot_scale)
    second = jnp.clip(0.985 * first + noise, -6.0 * hot_scale, 6.0 * hot_scale)
    base = base.at[:, first_cols].set(first)
    base = base.at[:, second_cols].set(second)
    return base


def draw_head(key, part):
    return head_matrix(key).astype(jnp.bfloat16)


def draw_hidden(key, part):
    base = jax.random.normal(jax.random.fold_in(key, 23), (SEQS, LEN, D), jnp.float32)
    first_cols, second_cols = hot_columns(key)
    which = jax.random.randint(jax.random.fold_in(key, 22), (SEQS, 4), 0, 4)
    columns = first_cols[which]
    picked = head_matrix(key)[:, columns]
    picked = jnp.transpose(picked, (1, 2, 0)) * (D / 160.0)
    base = base.at[:, :4, :].set(picked)
    return base.astype(jnp.bfloat16)


def plant(array, stream_key, low, top_value):
    dims = array.shape
    spot = [jax.random.randint(jax.random.fold_in(stream_key, axis), (), 0, dims[axis]) for axis in range(len(dims))]
    array = array.at[tuple(spot)].set(low)
    longest = dims.index(max(dims))
    spot[longest] = (spot[longest] + 1) % dims[longest]
    return array.at[tuple(spot)].set(top_value)


def choose_distinct(own_key, rows, count, top, lift):
    sequence = jax.random.permutation(jax.random.fold_in(own_key, 1), count)
    pull = sequence
    for power in range(3):
        pull = pull * pull // count
    pull = pull * lift // count
    tickets = jax.random.randint(jax.random.fold_in(own_key, 2), (rows, count), 0, 4096) + pull
    holders = jax.random.permutation(jax.random.fold_in(own_key, 3), rows)[jnp.arange(count) % rows]
    tickets = jnp.where(jnp.arange(rows)[:, None] == holders[None, :], 1 << 14, tickets)
    score = tickets * count + jnp.arange(count)
    return lax.top_k(score.astype(jnp.int32), top)[1].astype(jnp.int32)


def profile(amount, total, bound, slope):
    loads = [(1 << 20) // math.isqrt(rank ** slope) + 1 for rank in range(2, amount + 1)]
    surplus, given = total - bound - (amount - 1), [1] * (amount - 1)
    while surplus > 0:
        free = [i for i in range(amount - 1) if given[i] < bound]
        pool, left = sum([loads[i] for i in free]), surplus
        for i in free:
            more = min(bound - given[i], max(1, left * loads[i] // pool), surplus)
            given[i] = given[i] + more
            surplus = surplus - more
    return np.array([bound] + given)


def uneven_parts(rng, amount, total, reach, lean):
    if amount == 2:
        one = jax.random.randint(rng, (), max(1, total - reach), min(reach, total - 1) + 1)
        return jnp.stack([one, total - one])
    tallies = jnp.asarray(profile(amount, total, reach, lean), jnp.int32)
    pairs = (amount - 1) // 2
    giver, sink = tallies[1:1 + 2 * pairs:2], tallies[2:2 + 2 * pairs:2]
    margin = jnp.minimum(giver - 1, reach - sink)
    moved = jax.random.randint(jax.random.fold_in(rng, 1), (pairs,), 0, 1 << 20) % (margin + 1)
    tallies = tallies.at[1:1 + 2 * pairs:2].set(giver - moved).at[2:2 + 2 * pairs:2].set(sink + moved)
    return tallies[jax.random.permutation(jax.random.fold_in(rng, 2), amount)]


def setup_inputs(seed: int = 0) -> dict:
    streams_of = jax.random.split(jax.random.key(seed), 8)
    hidden = draw_hidden(jax.random.fold_in(streams_of[7], 71), 0)
    norm_gain = jnp.clip(1.0 + 0.1 * jax.random.normal(streams_of[1], (D,), jnp.float32), 0.5, 1.5)
    head = draw_head(jax.random.fold_in(streams_of[7], 71), 0)
    targets = plant(jax.random.randint(streams_of[3], (SEQS, LEN), 0, V), jax.random.fold_in(streams_of[3], 1), 0, V - 1).astype(jnp.int32)
    lengths = uneven_parts(streams_of[4], SEQS, TOTAL, LEN, 1).astype(jnp.int32)
    groups = choose_distinct(streams_of[5], SEQS, GROUPS, 1, 0)
    baseline = jnp.clip(jax.random.uniform(streams_of[6], (GROUPS,), jnp.float32, -2.0, 0.0), -2.0, 0.0)
    return dict(hidden=hidden, norm_gain=norm_gain, head=head, targets=targets, lengths=lengths, groups=groups, baseline=baseline)


def reference(hidden, norm_gain, head, targets, lengths, groups, baseline):
    total_rows = SEQS * LEN
    flat = hidden.reshape(total_rows, D).astype(jnp.float32)
    square = lax.optimization_barrier(jnp.mean(flat * flat, axis=-1, keepdims=True))
    normed = (flat * lax.rsqrt(square + 1e-05) * norm_gain.astype(jnp.float32)[None, :]).astype(jnp.bfloat16)
    picks = targets.reshape(total_rows)

    def block_stats(pair):
        rows, chosen_ids = pair
        logits = jnp.dot(rows, head, preferred_element_type=jnp.float32)
        top = lax.optimization_barrier(jnp.max(logits, axis=-1))
        shifted = logits - top[:, None]
        expo = jnp.exp(shifted)
        total = lax.optimization_barrier(jnp.sum(expo, axis=-1))
        spread = lax.optimization_barrier(jnp.sum(expo * shifted, axis=-1))
        chosen = jnp.take_along_axis(logits, chosen_ids[:, None], axis=1)[:, 0]
        return (chosen - top - jnp.log(total), jnp.log(total) - spread / total)
    logprob, entropy = lax.map(block_stats, (normed.reshape(SEQS, LEN, D), picks.reshape(SEQS, LEN)))
    positions = jnp.arange(LEN, dtype=jnp.int32)
    live = positions[None, :] < lengths[:, None]
    logprob = jnp.where(live, logprob, 0.0)
    entropy = jnp.where(live, entropy, 0.0)
    member = (groups[:, 0][:, None] == jnp.arange(GROUPS, dtype=jnp.int32)[None, :]).astype(jnp.float32)
    seq_sums = jnp.stack([lax.optimization_barrier(jnp.sum(logprob, axis=1)), lax.optimization_barrier(jnp.sum(entropy, axis=1)), lengths.astype(jnp.float32)], axis=1)
    group_sums = jnp.dot(member.T, seq_sums, precision=lax.Precision.HIGHEST)
    shift = jnp.stack([group_sums[:, 0] / group_sums[:, 2] - baseline, group_sums[:, 1] / group_sums[:, 2]], axis=0)
    return (logprob, entropy, shift)
```

```python
import jax
import jax.numpy as jnp
from jax import lax
from jax.sharding import PartitionSpec as P


def per_device(hidden, norm_gain, head, targets, lengths, groups, baseline):
    seq_count, slot_count, width = hidden.shape
    total_rows = seq_count * slot_count
    block = min(512, total_rows)
    weights = lax.all_gather(head, "dp", axis=0, tiled=True)
    vocab_width = weights.shape[1]
    offset = lax.axis_index("vocab") * vocab_width
    flat = hidden.reshape(total_rows, width).astype(jnp.float32)
    square = jnp.mean(flat * flat, axis=-1, keepdims=True)
    normed = (flat * lax.rsqrt(square + 1e-05) * norm_gain[None, :]).astype(jnp.bfloat16)
    positions = jnp.arange(slot_count, dtype=jnp.int32)
    live = (positions[None, :] < lengths[:, None]).reshape(total_rows)
    wanted = targets.reshape(total_rows)
    column = jnp.arange(vocab_width, dtype=jnp.int32) + offset

    def local_stats(rows, picks):
        logits = jnp.dot(rows, weights, preferred_element_type=jnp.float32)
        local_top = jnp.max(logits, axis=-1)
        shifted = logits - local_top[:, None]
        expo = jnp.exp(shifted)
        local_total = jnp.sum(expo, axis=-1)
        local_spread = jnp.sum(expo * shifted, axis=-1)
        chosen = jnp.sum(jnp.where(column[None, :] == picks[:, None], logits, 0.0), axis=-1)
        return jnp.stack([local_top, local_total, local_spread, chosen], axis=0)

    parts = [
        local_stats(normed[start : start + block], wanted[start : start + block])
        for start in range(0, total_rows, block)
    ]
    stats = jnp.concatenate(parts, axis=1)
    gathered = lax.all_gather(stats, "vocab", axis=0)
    tops = gathered[:, 0]
    top = jnp.max(tops, axis=0)
    factor = jnp.exp(tops - top[None, :])
    total = jnp.sum(gathered[:, 1] * factor, axis=0)
    spread = jnp.sum(factor * (gathered[:, 2] + gathered[:, 1] * (tops - top[None, :])), axis=0)
    target = jnp.sum(gathered[:, 3], axis=0)
    log_total = jnp.log(total)
    logprob = target - top - log_total
    entropy = log_total - spread / total
    logprob = jnp.where(live, logprob, 0.0).reshape(seq_count, slot_count)
    entropy = jnp.where(live, entropy, 0.0).reshape(seq_count, slot_count)
    group_count = baseline.shape[0]
    member = (groups[:, 0][:, None] == jnp.arange(group_count, dtype=jnp.int32)[None, :]).astype(
        jnp.float32
    )
    seq_sums = jnp.stack(
        [jnp.sum(logprob, axis=1), jnp.sum(entropy, axis=1), lengths.astype(jnp.float32)], axis=1
    )
    partial_value = jnp.dot(member.T, seq_sums, precision=lax.Precision.HIGHEST)
    group_value = jnp.sum(lax.all_gather(partial_value, "dp", axis=0), axis=0)
    group_lp, group_ent, group_cnt = group_value[:, 0], group_value[:, 1], group_value[:, 2]
    shift = jnp.stack([group_lp / group_cnt - baseline, group_ent / group_cnt], axis=0)
    return (logprob, entropy, shift)


def solution(mesh):
    placed = (
        P("dp", None, None),
        P(),
        P("dp", "vocab"),
        P("dp", None),
        P("dp"),
        P("dp", None),
        P(),
    )
    return jax.shard_map(
        per_device,
        mesh=mesh,
        in_specs=placed,
        out_specs=(P("dp", None), P("dp", None), P()),
        check_vma=False,
    )
```

```python
import jax
import jax.numpy as jnp
from jax import lax
from jax.sharding import PartitionSpec as P


def per_device(hidden, norm_gain, head, targets, lengths, groups, baseline):
    seq_count, slot_count, width = hidden.shape
    total_rows = seq_count * slot_count
    block = min(512, total_rows)
    weights = lax.all_gather(head, "dp", axis=0, tiled=True)
    vocab_width = weights.shape[1]
    offset = lax.axis_index("vocab") * vocab_width
    flat = hidden.reshape(total_rows, width).astype(jnp.float32)
    square = jnp.mean(flat * flat, axis=-1, keepdims=True)
    normed = (flat * lax.rsqrt(square + 1e-05) * norm_gain[None, :]).astype(jnp.bfloat16)
    positions = jnp.arange(slot_count, dtype=jnp.int32)
    live = (positions[None, :] < lengths[:, None]).reshape(total_rows)
    wanted = targets.reshape(total_rows)
    column = jnp.arange(vocab_width, dtype=jnp.int32) + offset

    def local_stats(rows, picks):
        logits = jnp.dot(rows, weights, preferred_element_type=jnp.float32)
        local_top = jnp.max(logits, axis=-1)
        shifted = logits - local_top[:, None]
        expo = jnp.exp(shifted)
        local_total = jnp.sum(expo, axis=-1)
        local_spread = jnp.sum(expo * shifted, axis=-1)
        chosen = jnp.sum(jnp.where(column[None, :] == picks[:, None], logits, 0.0), axis=-1)
        return jnp.stack([local_top, local_total, local_spread, chosen], axis=0)

    parts = [
        local_stats(normed[start : start + block], wanted[start : start + block])
        for start in range(0, total_rows, block)
    ]
    stats = jnp.concatenate(parts, axis=1)
    vocab_count = lax.axis_size("vocab")
    spread_out = jnp.broadcast_to(stats[None], (vocab_count,) + stats.shape)
    gathered = lax.all_to_all(spread_out, "vocab", 0, 0, tiled=False)
    tops = gathered[:, 0]
    top = jnp.max(tops, axis=0)
    factor = jnp.exp(tops - top[None, :])
    total = jnp.sum(gathered[:, 1] * factor, axis=0)
    spread = jnp.sum(factor * (gathered[:, 2] + gathered[:, 1] * (tops - top[None, :])), axis=0)
    target = jnp.sum(gathered[:, 3], axis=0)
    log_total = jnp.log(total)
    logprob = target - top - log_total
    entropy = log_total - spread / total
    logprob = jnp.where(live, logprob, 0.0).reshape(seq_count, slot_count)
    entropy = jnp.where(live, entropy, 0.0).reshape(seq_count, slot_count)
    group_count = baseline.shape[0]
    member = (groups[:, 0][:, None] == jnp.arange(group_count, dtype=jnp.int32)[None, :]).astype(
        jnp.float32
    )
    seq_sums = jnp.stack(
        [jnp.sum(logprob, axis=1), jnp.sum(entropy, axis=1), lengths.astype(jnp.float32)], axis=1
    )
    partial_value = jnp.dot(member.T, seq_sums, precision=lax.Precision.HIGHEST)
    dp_count = lax.axis_size("dp")
    partial_out = jnp.broadcast_to(partial_value[None], (dp_count,) + partial_value.shape)
    group_value = jnp.sum(lax.all_to_all(partial_out, "dp", 0, 0, tiled=False), axis=0)
    group_lp, group_ent, group_cnt = group_value[:, 0], group_value[:, 1], group_value[:, 2]
    shift = jnp.stack([group_lp / group_cnt - baseline, group_ent / group_cnt], axis=0)
    return (logprob, entropy, shift)


def solution(mesh):
    placed = (
        P("dp", None, None),
        P(),
        P("dp", "vocab"),
        P("dp", None),
        P("dp"),
        P("dp", None),
        P(),
    )
    return jax.shard_map(
        per_device,
        mesh=mesh,
        in_specs=placed,
        out_specs=(P("dp", None), P("dp", None), P()),
        check_vma=False,
    )
```

```python
import jax
import jax.numpy as jnp
from jax import lax
from jax.sharding import PartitionSpec as P


def per_device(hidden, norm_gain, head, targets, lengths, groups, baseline):
    seq_count, slot_count, width = hidden.shape
    total_rows = seq_count * slot_count
    block = total_rows
    weights = lax.all_gather(head, "dp", axis=0, tiled=True)
    vocab_width = weights.shape[1]
    offset = lax.axis_index("vocab") * vocab_width
    flat = hidden.reshape(total_rows, width).astype(jnp.float32)
    square = jnp.mean(flat * flat, axis=-1, keepdims=True)
    normed = (flat * lax.rsqrt(square + 1e-05) * norm_gain[None, :]).astype(jnp.bfloat16)
    positions = jnp.arange(slot_count, dtype=jnp.int32)
    live = (positions[None, :] < lengths[:, None]).reshape(total_rows)
    wanted = targets.reshape(total_rows)
    column = jnp.arange(vocab_width, dtype=jnp.int32) + offset

    def local_stats(rows, picks):
        logits = jnp.dot(rows, weights, preferred_element_type=jnp.float32)
        local_top = jnp.max(logits, axis=-1)
        shifted = logits - local_top[:, None]
        expo = jnp.exp(shifted)
        local_total = jnp.sum(expo, axis=-1)
        local_spread = jnp.sum(expo * shifted, axis=-1)
        chosen = jnp.sum(jnp.where(column[None, :] == picks[:, None], logits, 0.0), axis=-1)
        return jnp.stack([local_top, local_total, local_spread, chosen], axis=0)

    parts = [
        local_stats(normed[start : start + block], wanted[start : start + block])
        for start in range(0, total_rows, block)
    ]
    stats = jnp.concatenate(parts, axis=1)
    vocab_count = lax.axis_size("vocab")
    spread_out = jnp.broadcast_to(stats[None], (vocab_count,) + stats.shape)
    gathered = lax.all_to_all(spread_out, "vocab", 0, 0, tiled=False)
    tops = gathered[:, 0]
    top = jnp.max(tops, axis=0)
    factor = jnp.exp(tops - top[None, :])
    total = jnp.sum(gathered[:, 1] * factor, axis=0)
    spread = jnp.sum(factor * (gathered[:, 2] + gathered[:, 1] * (tops - top[None, :])), axis=0)
    target = jnp.sum(gathered[:, 3], axis=0)
    log_total = jnp.log(total)
    logprob = target - top - log_total
    entropy = log_total - spread / total
    logprob = jnp.where(live, logprob, 0.0).reshape(seq_count, slot_count)
    entropy = jnp.where(live, entropy, 0.0).reshape(seq_count, slot_count)
    group_count = baseline.shape[0]
    member = (groups[:, 0][:, None] == jnp.arange(group_count, dtype=jnp.int32)[None, :]).astype(
        jnp.float32
    )
    seq_sums = jnp.stack(
        [jnp.sum(logprob, axis=1), jnp.sum(entropy, axis=1), lengths.astype(jnp.float32)], axis=1
    )
    partial_value = jnp.dot(member.T, seq_sums, precision=lax.Precision.HIGHEST)
    dp_count = lax.axis_size("dp")
    partial_out = jnp.broadcast_to(partial_value[None], (dp_count,) + partial_value.shape)
    group_value = jnp.sum(lax.all_to_all(partial_out, "dp", 0, 0, tiled=False), axis=0)
    group_lp, group_ent, group_cnt = group_value[:, 0], group_value[:, 1], group_value[:, 2]
    shift = jnp.stack([group_lp / group_cnt - baseline, group_ent / group_cnt], axis=0)
    return (logprob, entropy, shift)


def solution(mesh):
    placed = (
        P("dp", None, None),
        P(),
        P("dp", "vocab"),
        P("dp", None),
        P("dp"),
        P("dp", None),
        P(),
    )
    return jax.shard_map(
        per_device,
        mesh=mesh,
        in_specs=placed,
        out_specs=(P("dp", None), P("dp", None), P()),
        check_vma=False,
    )
```

```python
import jax
import jax.numpy as jnp
from jax import lax
from jax.sharding import PartitionSpec as P


RING = 4
SLOTS = (0, 3, 1, 2)


def ring_step(pieces, along, step):
    def target(index):
        z, y = divmod(index, RING)
        if along == "z":
            return ((z + step) % RING) * RING + y
        return z * RING + (y + step) % RING

    return lax.ppermute(pieces, "dp", [(i, target(i)) for i in range(RING * RING)])


def ring_gather(block, along):
    from_before = ring_step(block, along, 1)
    from_after = ring_step(block, along, RING - 1)
    half = block.shape[0] // 2
    far = jnp.concatenate(
        [ring_step(from_before[:half], along, 1), ring_step(from_after[half:], along, RING - 1)], axis=0
    )
    return jnp.concatenate([block, from_before, from_after, far], axis=0)


def combine(stats):
    tops = stats[:, 0]
    top = jnp.max(tops, axis=0)
    factor = jnp.exp(tops - top[None, :])
    total = jnp.sum(stats[:, 1] * factor, axis=0)
    spread = jnp.sum(factor * (stats[:, 2] + stats[:, 1] * (tops - top[None, :])), axis=0)
    chosen = jnp.sum(stats[:, 3], axis=0)
    return jnp.stack([top, total, spread, chosen], axis=0)


def per_device(hidden, norm_gain, head, targets, lengths, groups, baseline):
    seq_count, slot_count, width = hidden.shape
    total_rows = seq_count * slot_count
    block = min(512, total_rows)
    vocab_width = head.shape[1]
    split = vocab_width // 2
    weights_a = ring_gather(ring_gather(head[:, :split], "z"), "y")
    weights_b = ring_gather(ring_gather(head[:, split:], "y"), "z")
    offset = lax.axis_index("vocab") * vocab_width
    here = lax.axis_index("dp")
    here_z, here_y = here // RING, here % RING
    flat = hidden.reshape(total_rows, width).astype(jnp.float32)
    square = jnp.mean(flat * flat, axis=-1, keepdims=True)
    normed = (flat * lax.rsqrt(square + 1e-05) * norm_gain[None, :]).astype(jnp.bfloat16)
    grid = normed.reshape(total_rows, RING, RING, width // (RING * RING))
    grid = jnp.roll(grid, (-here_z, -here_y), axis=(1, 2))
    order = jnp.array(SLOTS, dtype=jnp.int32)
    grid = jnp.take(jnp.take(grid, order, axis=1), order, axis=2)
    normed_b = grid.reshape(total_rows, width)
    normed_a = jnp.transpose(grid, (0, 2, 1, 3)).reshape(total_rows, width)
    positions = jnp.arange(slot_count, dtype=jnp.int32)
    live = (positions[None, :] < lengths[:, None]).reshape(total_rows)
    wanted = targets.reshape(total_rows)
    column = jnp.arange(vocab_width, dtype=jnp.int32) + offset

    def half_stats(rows, weights, picks, columns):
        logits = jnp.dot(rows, weights, preferred_element_type=jnp.float32)
        local_top = jnp.max(logits, axis=-1)
        shifted = logits - local_top[:, None]
        expo = jnp.exp(shifted)
        local_total = jnp.sum(expo, axis=-1)
        local_spread = jnp.sum(expo * shifted, axis=-1)
        chosen = jnp.sum(jnp.where(columns[None, :] == picks[:, None], logits, 0.0), axis=-1)
        return jnp.stack([local_top, local_total, local_spread, chosen], axis=0)

    def local_stats(start):
        picks = wanted[start : start + block]
        both = jnp.stack(
            [
                half_stats(normed_a[start : start + block], weights_a, picks, column[:split]),
                half_stats(normed_b[start : start + block], weights_b, picks, column[split:]),
            ],
            axis=0,
        )
        return combine(both)

    parts = [local_stats(start) for start in range(0, total_rows, block)]
    stats = jnp.concatenate(parts, axis=1)
    vocab_count = lax.axis_size("vocab")
    spread_out = jnp.broadcast_to(stats[None], (vocab_count,) + stats.shape)
    gathered = lax.all_to_all(spread_out, "vocab", 0, 0, tiled=False)
    top, total, spread, target = combine(gathered)
    log_total = jnp.log(total)
    logprob = target - top - log_total
    entropy = log_total - spread / total
    logprob = jnp.where(live, logprob, 0.0).reshape(seq_count, slot_count)
    entropy = jnp.where(live, entropy, 0.0).reshape(seq_count, slot_count)
    group_count = baseline.shape[0]
    member = (groups[:, 0][:, None] == jnp.arange(group_count, dtype=jnp.int32)[None, :]).astype(
        jnp.float32
    )
    seq_sums = jnp.stack(
        [jnp.sum(logprob, axis=1), jnp.sum(entropy, axis=1), lengths.astype(jnp.float32)], axis=1
    )
    partial_value = jnp.dot(member.T, seq_sums, precision=lax.Precision.HIGHEST)
    dp_count = lax.axis_size("dp")
    partial_out = jnp.broadcast_to(partial_value[None], (dp_count,) + partial_value.shape)
    group_value = jnp.sum(lax.all_to_all(partial_out, "dp", 0, 0, tiled=False), axis=0)
    group_lp, group_ent, group_cnt = group_value[:, 0], group_value[:, 1], group_value[:, 2]
    shift = jnp.stack([group_lp / group_cnt - baseline, group_ent / group_cnt], axis=0)
    return (logprob, entropy, shift)


def solution(mesh):
    placed = (
        P("dp", None, None),
        P(),
        P("dp", "vocab"),
        P("dp", None),
        P("dp"),
        P("dp", None),
        P(),
    )
    return jax.shard_map(
        per_device,
        mesh=mesh,
        in_specs=placed,
        out_specs=(P("dp", None), P("dp", None), P()),
        check_vma=False,
    )
```

```python
import functools

import jax
import jax.numpy as jnp
from jax import lax
from jax.experimental import pallas as pl
from jax.experimental.pallas import tpu as pltpu
from jax.sharding import PartitionSpec as P

LANE = 128
CHUNK = 512


def stats_kernel(x_ref, w_ref, p_ref, o_ref, *, valid):
    x = x_ref[...]
    picks = p_ref[...]
    rows, width = x.shape[0], w_ref.shape[1]
    top = total = spread = chosen = None
    for k in range(width // CHUNK):
        logits = jnp.dot(x, w_ref[:, k * CHUNK : (k + 1) * CHUNK], preferred_element_type=jnp.float32)
        cols = lax.broadcasted_iota(jnp.int32, (rows, CHUNK), 1) + k * CHUNK
        hit = jnp.sum(jnp.where(cols == picks, logits, 0.0), axis=1, keepdims=True)
        if (k + 1) * CHUNK > valid:
            logits = jnp.where(cols < valid, logits, -1e30)
        chunk_top = jnp.max(logits, axis=1, keepdims=True)
        if top is None:
            shifted = logits - chunk_top
            expo = jnp.exp(shifted)
            top, chosen = chunk_top, hit
            total = jnp.sum(expo, axis=1, keepdims=True)
            spread = jnp.sum(expo * shifted, axis=1, keepdims=True)
        else:
            new_top = jnp.maximum(top, chunk_top)
            factor = jnp.exp(top - new_top)
            shifted = logits - new_top
            expo = jnp.exp(shifted)
            spread = factor * (spread + total * (top - new_top)) + jnp.sum(expo * shifted, axis=1, keepdims=True)
            total = factor * total + jnp.sum(expo, axis=1, keepdims=True)
            top, chosen = new_top, chosen + hit
    o_ref[...] = jnp.concatenate([top, total, spread, chosen], axis=1)


def row_stats(rows, weights, picks, valid):
    count, width = rows.shape
    return pl.pallas_call(
        functools.partial(stats_kernel, valid=valid),
        grid=(1,),
        in_specs=[
            pl.BlockSpec((count, width), lambda i: (0, 0)),
            pl.BlockSpec(weights.shape, lambda i: (0, 0)),
            pl.BlockSpec((count, 1), lambda i: (0, 0)),
        ],
        out_specs=pl.BlockSpec((count, 4), lambda i: (0, 0)),
        out_shape=jax.ShapeDtypeStruct((count, 4), jnp.float32),
        compiler_params=pltpu.CompilerParams(vmem_limit_bytes=48 * 1024 * 1024),
    )(rows, weights, picks.reshape(count, 1))


def per_device(hidden, norm_gain, head, targets, lengths, groups, baseline):
    seq_count, slot_count, width = hidden.shape
    total_rows = seq_count * slot_count
    vocab_width = head.shape[1]
    padded = -(-vocab_width // CHUNK) * CHUNK
    weights = lax.all_gather(jnp.pad(head, ((0, 0), (0, padded - vocab_width))), "dp", axis=0, tiled=True)
    offset = lax.axis_index("vocab") * vocab_width
    flat = hidden.reshape(total_rows, width).astype(jnp.float32)
    square = jnp.mean(flat * flat, axis=-1, keepdims=True)
    normed = (flat * lax.rsqrt(square + 1e-05) * norm_gain[None, :]).astype(jnp.bfloat16)
    positions = jnp.arange(slot_count, dtype=jnp.int32)
    live = (positions[None, :] < lengths[:, None]).reshape(total_rows)
    wanted = targets.reshape(total_rows)
    stats = row_stats(normed, weights, wanted - offset, vocab_width).T
    vocab_count = lax.axis_size("vocab")
    spread_out = jnp.broadcast_to(stats[None], (vocab_count,) + stats.shape)
    gathered = lax.all_to_all(spread_out, "vocab", 0, 0, tiled=False)
    tops = gathered[:, 0]
    top = jnp.max(tops, axis=0)
    factor = jnp.exp(tops - top[None, :])
    total = jnp.sum(gathered[:, 1] * factor, axis=0)
    spread = jnp.sum(factor * (gathered[:, 2] + gathered[:, 1] * (tops - top[None, :])), axis=0)
    target = jnp.sum(gathered[:, 3], axis=0)
    log_total = jnp.log(total)
    logprob = target - top - log_total
    entropy = log_total - spread / total
    logprob = jnp.where(live, logprob, 0.0).reshape(seq_count, slot_count)
    entropy = jnp.where(live, entropy, 0.0).reshape(seq_count, slot_count)
    group_count = baseline.shape[0]
    member = (groups[:, 0][:, None] == jnp.arange(group_count, dtype=jnp.int32)[None, :]).astype(
        jnp.float32
    )
    seq_sums = jnp.stack(
        [jnp.sum(logprob, axis=1), jnp.sum(entropy, axis=1), lengths.astype(jnp.float32)], axis=1
    )
    partial_value = jnp.dot(member.T, seq_sums, precision=lax.Precision.HIGHEST)
    dp_count = lax.axis_size("dp")
    partial_out = jnp.broadcast_to(partial_value[None], (dp_count,) + partial_value.shape)
    group_value = jnp.sum(lax.all_to_all(partial_out, "dp", 0, 0, tiled=False), axis=0)
    group_lp, group_ent, group_cnt = group_value[:, 0], group_value[:, 1], group_value[:, 2]
    shift = jnp.stack([group_lp / group_cnt - baseline, group_ent / group_cnt], axis=0)
    return (logprob, entropy, shift)


def solution(mesh):
    placed = (
        P("dp", None, None),
        P(),
        P("dp", "vocab"),
        P("dp", None),
        P("dp"),
        P("dp", None),
        P(),
    )
    return jax.shard_map(
        per_device,
        mesh=mesh,
        in_specs=placed,
        out_specs=(P("dp", None), P("dp", None), P()),
        check_vma=False,
    )
```

```python
import functools

import jax
import jax.numpy as jnp
from jax import lax
from jax.experimental import pallas as pl
from jax.experimental.pallas import tpu as pltpu
from jax.sharding import PartitionSpec as P

LANE = 128
CHUNK = 256


def stats_kernel(x_ref, w_ref, p_ref, o_ref, *, valid):
    x = x_ref[...]
    picks = p_ref[...]
    rows, width = x.shape[0], w_ref.shape[1]
    top = total = spread = chosen = None
    for k in range(width // CHUNK):
        logits = jnp.dot(x, w_ref[:, k * CHUNK : (k + 1) * CHUNK], preferred_element_type=jnp.float32)
        cols = lax.broadcasted_iota(jnp.int32, (rows, CHUNK), 1) + k * CHUNK
        hit = jnp.sum(jnp.where(cols == picks, logits, 0.0), axis=1, keepdims=True)
        if (k + 1) * CHUNK > valid:
            logits = jnp.where(cols < valid, logits, -1e30)
        chunk_top = jnp.max(logits, axis=1, keepdims=True)
        if top is None:
            shifted = logits - chunk_top
            expo = jnp.exp(shifted)
            top, chosen = chunk_top, hit
            total = jnp.sum(expo, axis=1, keepdims=True)
            spread = jnp.sum(expo * shifted, axis=1, keepdims=True)
        else:
            new_top = jnp.maximum(top, chunk_top)
            factor = jnp.exp(top - new_top)
            shifted = logits - new_top
            expo = jnp.exp(shifted)
            spread = factor * (spread + total * (top - new_top)) + jnp.sum(expo * shifted, axis=1, keepdims=True)
            total = factor * total + jnp.sum(expo, axis=1, keepdims=True)
            top, chosen = new_top, chosen + hit
    o_ref[...] = jnp.concatenate([top, total, spread, chosen], axis=1)


def row_stats(rows, weights, picks, valid):
    count, width = rows.shape
    return pl.pallas_call(
        functools.partial(stats_kernel, valid=valid),
        grid=(1,),
        in_specs=[
            pl.BlockSpec((count, width), lambda i: (0, 0)),
            pl.BlockSpec(weights.shape, lambda i: (0, 0)),
            pl.BlockSpec((count, 1), lambda i: (0, 0)),
        ],
        out_specs=pl.BlockSpec((count, 4), lambda i: (0, 0)),
        out_shape=jax.ShapeDtypeStruct((count, 4), jnp.float32),
        compiler_params=pltpu.CompilerParams(vmem_limit_bytes=48 * 1024 * 1024),
    )(rows, weights, picks.reshape(count, 1))


def per_device(hidden, norm_gain, head, targets, lengths, groups, baseline):
    seq_count, slot_count, width = hidden.shape
    total_rows = seq_count * slot_count
    vocab_width = head.shape[1]
    padded = -(-vocab_width // CHUNK) * CHUNK
    weights = lax.all_gather(jnp.pad(head, ((0, 0), (0, padded - vocab_width))), "dp", axis=0, tiled=True)
    offset = lax.axis_index("vocab") * vocab_width
    flat = hidden.reshape(total_rows, width).astype(jnp.float32)
    square = jnp.mean(flat * flat, axis=-1, keepdims=True)
    normed = (flat * lax.rsqrt(square + 1e-05) * norm_gain[None, :]).astype(jnp.bfloat16)
    positions = jnp.arange(slot_count, dtype=jnp.int32)
    live = (positions[None, :] < lengths[:, None]).reshape(total_rows)
    wanted = targets.reshape(total_rows)
    stats = row_stats(normed, weights, wanted - offset, vocab_width).T
    vocab_count = lax.axis_size("vocab")
    spread_out = jnp.broadcast_to(stats[None], (vocab_count,) + stats.shape)
    gathered = lax.all_to_all(spread_out, "vocab", 0, 0, tiled=False)
    tops = gathered[:, 0]
    top = jnp.max(tops, axis=0)
    factor = jnp.exp(tops - top[None, :])
    total = jnp.sum(gathered[:, 1] * factor, axis=0)
    spread = jnp.sum(factor * (gathered[:, 2] + gathered[:, 1] * (tops - top[None, :])), axis=0)
    target = jnp.sum(gathered[:, 3], axis=0)
    log_total = jnp.log(total)
    logprob = target - top - log_total
    entropy = log_total - spread / total
    logprob = jnp.where(live, logprob, 0.0).reshape(seq_count, slot_count)
    entropy = jnp.where(live, entropy, 0.0).reshape(seq_count, slot_count)
    group_count = baseline.shape[0]
    member = (groups[:, 0][:, None] == jnp.arange(group_count, dtype=jnp.int32)[None, :]).astype(
        jnp.float32
    )
    seq_sums = jnp.stack(
        [jnp.sum(logprob, axis=1), jnp.sum(entropy, axis=1), lengths.astype(jnp.float32)], axis=1
    )
    partial_value = jnp.dot(member.T, seq_sums, precision=lax.Precision.HIGHEST)
    dp_count = lax.axis_size("dp")
    partial_out = jnp.broadcast_to(partial_value[None], (dp_count,) + partial_value.shape)
    group_value = jnp.sum(lax.all_to_all(partial_out, "dp", 0, 0, tiled=False), axis=0)
    group_lp, group_ent, group_cnt = group_value[:, 0], group_value[:, 1], group_value[:, 2]
    shift = jnp.stack([group_lp / group_cnt - baseline, group_ent / group_cnt], axis=0)
    return (logprob, entropy, shift)


def solution(mesh):
    placed = (
        P("dp", None, None),
        P(),
        P("dp", "vocab"),
        P("dp", None),
        P("dp"),
        P("dp", None),
        P(),
    )
    return jax.shard_map(
        per_device,
        mesh=mesh,
        in_specs=placed,
        out_specs=(P("dp", None), P("dp", None), P()),
        check_vma=False,
    )
```

```python
import functools

import jax
import jax.numpy as jnp
from jax import lax
from jax.experimental import pallas as pl
from jax.experimental.pallas import tpu as pltpu
from jax.sharding import PartitionSpec as P

LANE = 128
CHUNK = 256


def stats_kernel(x_ref, w_ref, p_ref, o_ref, *, valid):
    x = x_ref[...]
    picks = p_ref[...]
    rows, width = x.shape[0], w_ref.shape[1]
    top = total = spread = chosen = None
    for k in range(width // CHUNK):
        logits = jnp.dot(x, w_ref[:, k * CHUNK : (k + 1) * CHUNK], preferred_element_type=jnp.float32)
        cols = lax.broadcasted_iota(jnp.int32, (rows, CHUNK), 1) + k * CHUNK
        hit = jnp.sum(jnp.where(cols == picks, logits, 0.0), axis=1, keepdims=True)
        if (k + 1) * CHUNK > valid:
            logits = jnp.where(cols < valid, logits, -1e30)
        chunk_top = jnp.max(logits, axis=1, keepdims=True)
        if top is None:
            shifted = logits - chunk_top
            expo = jnp.exp(shifted)
            top, chosen = chunk_top, hit
            total = jnp.sum(expo, axis=1, keepdims=True)
            spread = jnp.sum(expo * shifted, axis=1, keepdims=True)
        else:
            new_top = jnp.maximum(top, chunk_top)
            factor = jnp.exp(top - new_top)
            shifted = logits - new_top
            expo = jnp.exp(shifted)
            spread = factor * (spread + total * (top - new_top)) + jnp.sum(expo * shifted, axis=1, keepdims=True)
            total = factor * total + jnp.sum(expo, axis=1, keepdims=True)
            top, chosen = new_top, chosen + hit
    o_ref[...] = jnp.concatenate([top, total, spread, chosen], axis=1)


def row_stats(rows, weights, picks, valid):
    count, width = rows.shape
    return pl.pallas_call(
        functools.partial(stats_kernel, valid=valid),
        grid=(1,),
        in_specs=[
            pl.BlockSpec((count, width), lambda i: (0, 0)),
            pl.BlockSpec(weights.shape, lambda i: (0, 0)),
            pl.BlockSpec((count, 1), lambda i: (0, 0)),
        ],
        out_specs=pl.BlockSpec((count, 4), lambda i: (0, 0)),
        out_shape=jax.ShapeDtypeStruct((count, 4), jnp.float32),
        compiler_params=pltpu.CompilerParams(vmem_limit_bytes=48 * 1024 * 1024),
    )(rows, weights, picks.reshape(count, 1))


def per_device(hidden, norm_gain, head, targets, lengths, groups, baseline):
    seq_count, slot_count, width = hidden.shape
    total_rows = seq_count * slot_count
    vocab_width = head.shape[1]
    padded = -(-vocab_width // CHUNK) * CHUNK
    weights = lax.all_gather(jnp.pad(head, ((0, 0), (0, padded - vocab_width))), "dp", axis=0, tiled=True)
    offset = lax.axis_index("vocab") * vocab_width
    flat = hidden.reshape(total_rows, width).astype(jnp.float32)
    square = jnp.mean(flat * flat, axis=-1, keepdims=True)
    normed = (flat * lax.rsqrt(square + 1e-05) * norm_gain[None, :]).astype(jnp.bfloat16)
    positions = jnp.arange(slot_count, dtype=jnp.int32)
    live = (positions[None, :] < lengths[:, None]).reshape(total_rows)
    wanted = targets.reshape(total_rows)
    stats = row_stats(normed, weights, wanted - offset, vocab_width).T
    vocab_count = lax.axis_size("vocab")
    spread_out = jnp.broadcast_to(stats[None], (vocab_count,) + stats.shape)
    gathered = lax.all_to_all(spread_out, "vocab", 0, 0, tiled=False)
    tops = gathered[:, 0]
    top = jnp.max(tops, axis=0)
    factor = jnp.exp(tops - top[None, :])
    total = jnp.sum(gathered[:, 1] * factor, axis=0)
    spread = jnp.sum(factor * (gathered[:, 2] + gathered[:, 1] * (tops - top[None, :])), axis=0)
    target = jnp.sum(gathered[:, 3], axis=0)
    log_total = jnp.log(total)
    logprob = target - top - log_total
    entropy = log_total - spread / total
    logprob = jnp.where(live, logprob, 0.0).reshape(seq_count, slot_count)
    entropy = jnp.where(live, entropy, 0.0).reshape(seq_count, slot_count)
    group_count = baseline.shape[0]
    member = (groups[:, 0][:, None] == jnp.arange(group_count, dtype=jnp.int32)[None, :]).astype(
        jnp.float32
    )
    seq_sums = jnp.stack(
        [jnp.sum(logprob, axis=1), jnp.sum(entropy, axis=1), lengths.astype(jnp.float32)], axis=1
    )
    partial_value = jnp.dot(member.T, seq_sums, precision=lax.Precision.HIGHEST)
    dp_count = lax.axis_size("dp")
    flat_value = partial_value.reshape(1, -1)
    partial_out = jnp.broadcast_to(flat_value, (dp_count, flat_value.shape[1]))
    summed = jnp.sum(lax.all_to_all(partial_out, "dp", 0, 0, tiled=True), axis=0)
    group_value = summed.reshape(partial_value.shape)
    group_lp, group_ent, group_cnt = group_value[:, 0], group_value[:, 1], group_value[:, 2]
    shift = jnp.stack([group_lp / group_cnt - baseline, group_ent / group_cnt], axis=0)
    return (logprob, entropy, shift)


def solution(mesh):
    placed = (
        P("dp", None, None),
        P(),
        P("dp", "vocab"),
        P("dp", None),
        P("dp"),
        P("dp", None),
        P(),
    )
    return jax.shard_map(
        per_device,
        mesh=mesh,
        in_specs=placed,
        out_specs=(P("dp", None), P("dp", None), P()),
        check_vma=False,
    )
```

```python
import functools

import jax
import jax.numpy as jnp
from jax import lax
from jax.experimental import pallas as pl
from jax.experimental.pallas import tpu as pltpu
from jax.sharding import PartitionSpec as P

CHUNK = 512


def stats_kernel(x_ref, w_ref, p_ref, o_ref, *, valid):
    x = x_ref[...]
    picks = p_ref[...]
    rows, width = x.shape[0], w_ref.shape[1]
    top = total = spread = chosen = None
    for k in range(width // CHUNK):
        logits = lax.dot_general(
            w_ref[:, k * CHUNK : (k + 1) * CHUNK], x, (((0,), (1,)), ((), ())), preferred_element_type=jnp.float32
        )
        cols = lax.broadcasted_iota(jnp.int32, (CHUNK, rows), 0) + k * CHUNK
        hit = jnp.sum(jnp.where(cols == picks, logits, 0.0), axis=0, keepdims=True)
        if (k + 1) * CHUNK > valid:
            logits = jnp.where(cols < valid, logits, -1e30)
        chunk_top = jnp.max(logits, axis=0, keepdims=True)
        if top is None:
            shifted = logits - chunk_top
            expo = jnp.exp(shifted)
            top, chosen = chunk_top, hit
            total = jnp.sum(expo, axis=0, keepdims=True)
            spread = jnp.sum(expo * shifted, axis=0, keepdims=True)
        else:
            new_top = jnp.maximum(top, chunk_top)
            factor = jnp.exp(top - new_top)
            shifted = logits - new_top
            expo = jnp.exp(shifted)
            spread = factor * (spread + total * (top - new_top)) + jnp.sum(expo * shifted, axis=0, keepdims=True)
            total = factor * total + jnp.sum(expo, axis=0, keepdims=True)
            top, chosen = new_top, chosen + hit
    block = jnp.concatenate([top, total, spread, chosen], axis=0)
    for peer in range(o_ref.shape[0]):
        o_ref[peer] = block


def row_stats(rows, weights, picks, valid, peers):
    count, width = rows.shape
    return pl.pallas_call(
        functools.partial(stats_kernel, valid=valid),
        grid=(1,),
        in_specs=[
            pl.BlockSpec((count, width), lambda i: (0, 0)),
            pl.BlockSpec(weights.shape, lambda i: (0, 0)),
            pl.BlockSpec((1, count), lambda i: (0, 0)),
        ],
        out_specs=pl.BlockSpec((peers, 4, count), lambda i: (0, 0, 0)),
        out_shape=jax.ShapeDtypeStruct((peers, 4, count), jnp.float32),
        compiler_params=pltpu.CompilerParams(vmem_limit_bytes=48 * 1024 * 1024),
    )(rows, weights, picks.reshape(1, count))


def per_device(hidden, norm_gain, head, targets, lengths, groups, baseline):
    seq_count, slot_count, width = hidden.shape
    total_rows = seq_count * slot_count
    vocab_width = head.shape[1]
    padded = -(-vocab_width // CHUNK) * CHUNK
    weights = lax.all_gather(jnp.pad(head, ((0, 0), (0, padded - vocab_width))), "dp", axis=0, tiled=True)
    offset = lax.axis_index("vocab") * vocab_width
    flat = hidden.reshape(total_rows, width).astype(jnp.float32)
    square = jnp.mean(flat * flat, axis=-1, keepdims=True)
    normed = (flat * lax.rsqrt(square + 1e-05) * norm_gain[None, :]).astype(jnp.bfloat16)
    positions = jnp.arange(slot_count, dtype=jnp.int32)
    live = (positions[None, :] < lengths[:, None]).reshape(total_rows)
    wanted = targets.reshape(total_rows)
    vocab_count = lax.axis_size("vocab")
    spread_out = row_stats(normed, weights, wanted - offset, vocab_width, vocab_count)
    gathered = lax.all_to_all(spread_out, "vocab", 0, 0, tiled=False)
    tops = gathered[:, 0]
    top = jnp.max(tops, axis=0)
    factor = jnp.exp(tops - top[None, :])
    total = jnp.sum(gathered[:, 1] * factor, axis=0)
    spread = jnp.sum(factor * (gathered[:, 2] + gathered[:, 1] * (tops - top[None, :])), axis=0)
    target = jnp.sum(gathered[:, 3], axis=0)
    log_total = jnp.log(total)
    logprob = target - top - log_total
    entropy = log_total - spread / total
    logprob = jnp.where(live, logprob, 0.0).reshape(seq_count, slot_count)
    entropy = jnp.where(live, entropy, 0.0).reshape(seq_count, slot_count)
    group_count = baseline.shape[0]
    member = (groups[:, 0][:, None] == jnp.arange(group_count, dtype=jnp.int32)[None, :]).astype(
        jnp.float32
    )
    seq_sums = jnp.stack(
        [jnp.sum(logprob, axis=1), jnp.sum(entropy, axis=1), lengths.astype(jnp.float32)], axis=1
    )
    partial_value = jnp.dot(member.T, seq_sums, precision=lax.Precision.HIGHEST)
    dp_count = lax.axis_size("dp")
    partial_out = jnp.broadcast_to(partial_value[None], (dp_count,) + partial_value.shape)
    group_value = jnp.sum(lax.all_to_all(partial_out, "dp", 0, 0, tiled=False), axis=0)
    group_lp, group_ent, group_cnt = group_value[:, 0], group_value[:, 1], group_value[:, 2]
    shift = jnp.stack([group_lp / group_cnt - baseline, group_ent / group_cnt], axis=0)
    return (logprob, entropy, shift)


def solution(mesh):
    placed = (
        P("dp", None, None),
        P(),
        P("dp", "vocab"),
        P("dp", None),
        P("dp"),
        P("dp", None),
        P(),
    )
    return jax.shard_map(
        per_device,
        mesh=mesh,
        in_specs=placed,
        out_specs=(P("dp", None), P("dp", None), P()),
        check_vma=False,
    )
```
